32 devices in a mesh: grp: 4 (over z), shard: 8 (over y, x, core).
Axes of the slice: x: 2, y: 2, z: 4, core: 2. Of those that a mesh axis runs over, the one named last changes fastest.
Arguments:
- points: bfloat16 [65536, 768], P(('grp', 'shard')), may hold values from -6 to 6
- local_ids: int32 [65536], P(('grp', 'shard')), may hold values from 0 to 2047
- block_counts: int32 [32, 32], P(('grp', 'shard')), may hold values from 0 to 64, as said below
- centroids: float32 [65536, 768], P(('grp', 'shard')), may hold values from -6 to 6
- counts: float32 [65536], P(('grp', 'shard')), may hold values from 1 to 8
- queries: bfloat16 [1024, 768], P(('grp', 'shard')), may hold values from -6 to 6
Outputs:
- updated: float32 [65536, 768], P(('grp', 'shard'))
- new_counts: float32 [65536], P(('grp', 'shard'))
- distance: float32 [1024], P(('grp', 'shard'))
The draws below stay inside these ranges and needn't reach their ends.
Inputs may be any that keep to these rules, and one draw needn't show every extreme that they name: block_counts[d, o] counts the occupied slots at the start of owner o's block in device d's buffer; the other slots of the block are padding whose points and ids matter to nothing. Some owner block is full in every device's buffer, and some owner receives full blocks from every device. `local_ids`: an index within the owning device's block of 2048 centroids.
All inputs are finite; a program needn't handle non-finite values.
Results may differ from the reference program's by a relative error of at most 0.0003.
Values may be sent and summed in bfloat16 or wider, within the bound.
No kernel may reach another device: no remote copies, remote signals or barrier semaphores. Data moves between devices by JAX's collectives and lax.ppermute only.
A program may use at most 128 MiB of HBM per device.

```python
import math
import jax
import jax.numpy as jnp
from jax import lax

D = 768
K_OWN = 2048
SLOTS_DEV = 2048
OWNERS = 32
CAP = 64
K = 65536
Q_ALL = 1024


def draw_block_counts(key, part):
    keys = jax.random.split(jax.random.fold_in(key, 17), 5)
    base_fill = jax.random.randint(keys[0], (OWNERS, OWNERS), 0, CAP + 1)
    heavy_owner = jax.random.randint(keys[1], (OWNERS,), 0, 8) == 0
    heavy_fill = jax.random.randint(keys[2], (OWNERS, OWNERS), CAP // 2, CAP + 1)
    filled = jnp.where(heavy_owner[None, :], heavy_fill, base_fill)
    column = jnp.arange(OWNERS, dtype=jnp.int32)[None, :]
    full_owner = jax.random.randint(keys[3], (), 0, OWNERS)
    filled = jnp.where(column == full_owner, CAP, filled)
    row_full = jax.random.randint(keys[4], (OWNERS,), 0, OWNERS)
    filled = jnp.where(column == row_full[:, None], CAP, filled)
    return filled.astype(jnp.int32)


def plant(result, own_key, least, top_value):
    dims = result.shape
    spot = [jax.random.randint(jax.random.fold_in(own_key, axis), (), 0, dims[axis]) for axis in range(len(dims))]
    result = result.at[tuple(spot)].set(least)
    longest = dims.index(max(dims))
    spot[longest] = (spot[longest] + 1) % dims[longest]
    return result.at[tuple(spot)].set(top_value)


def levels(own_key, shape, cuts, low, high):
    gain, own = 1.0, jax.random.fold_in(own_key, 6)
    for dim, parts in cuts:
        draws = jnp.exp(jax.random.uniform(jax.random.fold_in(own, dim), (parts,), jnp.float32, low / len(cuts), high / len(cuts)))
        gain = gain * jnp.repeat(draws, shape[dim] // parts).reshape([-1 if axis == dim else 1 for axis in range(len(shape))])
    return gain


def centred(own_key, shape, deviation, reach, cuts=(), kind=jnp.bfloat16):
    result = jax.random.normal(own_key, shape, jnp.float32) * deviation
    if len(cuts) > 0:
        result = levels(own_key, shape, cuts, -0.22, 0.18) * result
    return jnp.clip(result, min=-reach, max=reach).astype(kind)


def setup_inputs(seed: int = 0) -> dict:
    key_of = jax.random.split(jax.random.key(seed), 7)
    points = centred(key_of[0], (OWNERS * SLOTS_DEV, D), 1.0, 6.0, ((0, 32),))
    local_ids = plant(jax.random.randint(key_of[1], (OWNERS * SLOTS_DEV,), 0, K_OWN), jax.random.fold_in(key_of[1], 1), 0, K_OWN - 1).astype(jnp.int32)
    block_counts = draw_block_counts(jax.random.fold_in(key_of[6], 71), 0)
    centroids = centred(key_of[3], (K, D), 1.0, 6.0, ((0, 32),), jnp.float32)
    counts = jnp.clip(jnp.exp(math.log(8.0) - 2.0794415 * jax.random.uniform(key_of[4], (K,), jnp.float32) ** levels(key_of[4], (K,), ((0, 32),), -0.2, 0.2)), 1.0, 8.0)
    queries = centred(key_of[5], (Q_ALL, D), 1.0, 6.0, ((0, 32),))
    return dict(points=points, local_ids=local_ids, block_counts=block_counts, centroids=centroids, counts=counts, queries=queries)


def reference(points, local_ids, block_counts, centroids, counts, queries):
    capacity = SLOTS_DEV // OWNERS
    routed = points.reshape(OWNERS, OWNERS, capacity, D)
    slot_index = jnp.arange(capacity, dtype=jnp.int32)
    occupied = slot_index[None, None, :] < block_counts[:, :, None]
    target = jnp.where(occupied, local_ids.reshape(OWNERS, OWNERS, capacity), K_OWN).astype(jnp.int32)

    def per_owner(owner):
        owner_rows = lax.dynamic_index_in_dim(routed, owner, 1, keepdims=False).reshape(OWNERS * capacity, D)
        owner_ids = lax.dynamic_index_in_dim(target, owner, 1, keepdims=False).reshape(OWNERS * capacity)
        owner_sums = jax.ops.segment_sum(owner_rows.astype(jnp.float32), owner_ids, num_segments=K_OWN + 1)
        owner_hits = jax.ops.segment_sum(jnp.ones((OWNERS * capacity,), jnp.float32), owner_ids, num_segments=K_OWN + 1)
        return owner_sums[:K_OWN], owner_hits[:K_OWN]

    row_sums, hits = lax.map(per_owner, jnp.arange(OWNERS, dtype=jnp.int32))
    row_sums = row_sums.reshape(K, D)
    hits = hits.reshape(K)
    new_counts = counts + hits
    updated = centroids + (row_sums - hits[:, None] * centroids) / new_counts[:, None]
    rounded = updated.astype(jnp.bfloat16)
    query_norm = jnp.sum(jnp.square(queries.astype(jnp.float32)), axis=1)

    def fold_min(running, cent_block):
        inner = lax.dot_general(queries, cent_block, (((1,), (1,)), ((), ())), preferred_element_type=jnp.float32)
        cent_norm = jnp.sum(jnp.square(cent_block.astype(jnp.float32)), axis=1)
        return jnp.minimum(running, jnp.min(cent_norm[None, :] - 2.0 * inner, axis=1)), None

    start_min = jnp.full((Q_ALL,), jnp.inf, jnp.float32)
    running, _ = lax.scan(fold_min, start_min, rounded.reshape(OWNERS, K_OWN, D))
    distance = (running + query_norm) / D
    return updated, new_counts, distance
```

```python
import functools

import jax
import jax.numpy as jnp
from jax import lax
from jax.experimental import pallas as pl
from jax.experimental.pallas import tpu as pltpu
from jax.sharding import PartitionSpec as P


def fused_kernel(ids_ref, rows_ref, cent_ref, counts_ref, q_ref, upd_ref, nc_ref, min_ref, *, tile):
    step = pl.program_id(0)
    centroid = step * tile + lax.broadcasted_iota(jnp.int32, (tile, 1), 0)
    match = ids_ref[...] == centroid
    onehot = jnp.where(match, 1.0, 0.0)
    sums = jnp.dot(
        onehot.astype(jnp.bfloat16), rows_ref[...], preferred_element_type=jnp.float32
    )
    hits = jnp.sum(onehot, axis=1, keepdims=True)
    cent = cent_ref[...]
    new_counts = counts_ref[...] + hits
    updated = cent + (sums - hits * cent) / new_counts
    upd_ref[...] = updated
    nc_ref[...] = new_counts
    rounded = updated.astype(jnp.bfloat16)
    wide = rounded.astype(jnp.float32)
    norm = jnp.sum(wide * wide, axis=1, keepdims=True)
    inner = lax.dot_general(
        rounded, q_ref[...], (((1,), (1,)), ((), ())), preferred_element_type=jnp.float32
    )
    least = jnp.min(norm - 2.0 * inner, axis=0, keepdims=True)

    @pl.when(step == 0)
    def _():
        min_ref[...] = least

    @pl.when(step > 0)
    def _():
        min_ref[...] = jnp.minimum(min_ref[...], least)


def fused_update(ids_row, rows, centroids, counts_col, all_queries, tile):
    owned, features = centroids.shape
    slots = rows.shape[0]
    query_all = all_queries.shape[0]
    steps = owned // tile
    flops = 2 * owned * slots * features + 2 * owned * query_all * features
    moved = rows.size * 2 + centroids.size * 8 + all_queries.size * 2
    return pl.pallas_call(
        functools.partial(fused_kernel, tile=tile),
        grid=(steps,),
        in_specs=[
            pl.BlockSpec((1, slots), lambda i: (0, 0)),
            pl.BlockSpec((slots, features), lambda i: (0, 0)),
            pl.BlockSpec((tile, features), lambda i: (i, 0)),
            pl.BlockSpec((tile, 1), lambda i: (i, 0)),
            pl.BlockSpec((query_all, features), lambda i: (0, 0)),
        ],
        out_specs=[
            pl.BlockSpec((tile, features), lambda i: (i, 0)),
            pl.BlockSpec((tile, 1), lambda i: (i, 0)),
            pl.BlockSpec((1, query_all), lambda i: (0, 0)),
        ],
        out_shape=[
            jax.ShapeDtypeStruct((owned, features), jnp.float32),
            jax.ShapeDtypeStruct((owned, 1), jnp.float32),
            jax.ShapeDtypeStruct((1, query_all), jnp.float32),
        ],
        compiler_params=pltpu.CompilerParams(
            dimension_semantics=("arbitrary",), vmem_limit_bytes=60 * 1024 * 1024
        ),
        cost_estimate=pl.CostEstimate(flops=flops, bytes_accessed=moved, transcendentals=0),
    )(ids_row, rows, centroids, counts_col, all_queries)


def body(points, local_ids, block_counts, centroids, counts, queries):
    groups = lax.axis_size("grp")
    shards = lax.axis_size("shard")
    owners = groups * shards
    slot_rows, features = points.shape
    capacity = slot_rows // owners
    owned = centroids.shape[0]
    query_rows = queries.shape[0]
    position = lax.broadcasted_iota(jnp.int32, (owners, capacity), 1)
    filled = block_counts.reshape(owners, 1)
    tagged = jnp.where(position < filled, local_ids.reshape(owners, capacity), -1).reshape(
        slot_rows
    )
    arrived = lax.all_to_all(points, ("grp", "shard"), split_axis=0, concat_axis=0, tiled=True)
    arrived_ids = lax.all_to_all(tagged, ("grp", "shard"), split_axis=0, concat_axis=0, tiled=True)
    all_queries = lax.all_gather(queries, ("grp", "shard"), axis=0, tiled=True)
    tile = 256 if owned % 256 == 0 else owned
    updated, new_counts, partial = fused_update(
        arrived_ids.reshape(1, slot_rows),
        arrived,
        centroids,
        counts.reshape(owned, 1),
        all_queries,
        tile,
    )
    gathered = lax.all_to_all(
        partial.reshape(owners, query_rows), ("grp", "shard"), split_axis=0, concat_axis=0,
        tiled=True,
    )
    own_best = jnp.min(gathered, axis=0)
    query_norm = jnp.sum(jnp.square(queries.astype(jnp.float32)), axis=1)
    distance = (own_best + query_norm) / features
    return (updated, new_counts.reshape(owned), distance)


def solution(mesh):
    placed = (
        P(("grp", "shard"), None),
        P(("grp", "shard")),
        P(("grp", "shard"), None),
        P(("grp", "shard"), None),
        P(("grp", "shard")),
        P(("grp", "shard"), None),
    )
    return jax.shard_map(
        body,
        mesh=mesh,
        in_specs=placed,
        out_specs=(P(("grp", "shard"), None), P(("grp", "shard")), P(("grp", "shard"))),
        check_vma=False,
    )
```

```python
import functools

import jax
import jax.numpy as jnp
from jax import lax
from jax.experimental import pallas as pl
from jax.experimental.pallas import tpu as pltpu
from jax.sharding import PartitionSpec as P


def fused_kernel(ids_ref, rows_ref, cent_ref, counts_ref, q_ref, upd_ref, nc_ref, min_ref, *, tile):
    step = pl.program_id(0)
    centroid = step * tile + lax.broadcasted_iota(jnp.int32, (tile, 1), 0)
    match = ids_ref[...] == centroid
    onehot = jnp.where(match, 1.0, 0.0)
    sums = jnp.dot(
        onehot.astype(jnp.bfloat16), rows_ref[...], preferred_element_type=jnp.float32
    )
    hits = jnp.sum(onehot, axis=1, keepdims=True)
    cent = cent_ref[...]
    new_counts = counts_ref[...] + hits
    updated = cent + (sums - hits * cent) / new_counts
    upd_ref[...] = updated
    nc_ref[...] = new_counts
    rounded = updated.astype(jnp.bfloat16)
    wide = rounded.astype(jnp.float32)
    norm = jnp.sum(wide * wide, axis=1, keepdims=True)
    inner = lax.dot_general(
        rounded, q_ref[...], (((1,), (1,)), ((), ())), preferred_element_type=jnp.float32
    )
    least = jnp.min(norm - 2.0 * inner, axis=0, keepdims=True)

    @pl.when(step == 0)
    def _():
        min_ref[...] = least

    @pl.when(step > 0)
    def _():
        min_ref[...] = jnp.minimum(min_ref[...], least)


def fused_update(ids_row, rows, centroids, counts_col, all_queries, tile):
    owned, features = centroids.shape
    slots = rows.shape[0]
    query_all = all_queries.shape[0]
    steps = owned // tile
    flops = 2 * owned * slots * features + 2 * owned * query_all * features
    moved = rows.size * 2 + centroids.size * 8 + all_queries.size * 2
    return pl.pallas_call(
        functools.partial(fused_kernel, tile=tile),
        grid=(steps,),
        in_specs=[
            pl.BlockSpec((1, slots), lambda i: (0, 0)),
            pl.BlockSpec((slots, features), lambda i: (0, 0)),
            pl.BlockSpec((tile, features), lambda i: (i, 0)),
            pl.BlockSpec((tile, 1), lambda i: (i, 0)),
            pl.BlockSpec((query_all, features), lambda i: (0, 0)),
        ],
        out_specs=[
            pl.BlockSpec((tile, features), lambda i: (i, 0)),
            pl.BlockSpec((tile, 1), lambda i: (i, 0)),
            pl.BlockSpec((1, query_all), lambda i: (0, 0)),
        ],
        out_shape=[
            jax.ShapeDtypeStruct((owned, features), jnp.float32),
            jax.ShapeDtypeStruct((owned, 1), jnp.float32),
            jax.ShapeDtypeStruct((1, query_all), jnp.float32),
        ],
        compiler_params=pltpu.CompilerParams(
            dimension_semantics=("arbitrary",), vmem_limit_bytes=60 * 1024 * 1024
        ),
        cost_estimate=pl.CostEstimate(flops=flops, bytes_accessed=moved, transcendentals=0),
    )(ids_row, rows, centroids, counts_col, all_queries)


def body(points, local_ids, block_counts, centroids, counts, queries):
    groups = lax.axis_size("grp")
    shards = lax.axis_size("shard")
    owners = groups * shards
    slot_rows, features = points.shape
    capacity = slot_rows // owners
    owned = centroids.shape[0]
    query_rows = queries.shape[0]
    position = lax.broadcasted_iota(jnp.int32, (owners, capacity), 1)
    filled = block_counts.reshape(owners, 1)
    tagged = jnp.where(position < filled, local_ids.reshape(owners, capacity), -1).reshape(
        slot_rows
    )
    arrived = lax.all_to_all(points, ("grp", "shard"), split_axis=0, concat_axis=0, tiled=True)
    every_ids = lax.all_gather(tagged.reshape(owners, capacity), ("grp", "shard"), axis=0)
    arrived_ids = lax.dynamic_index_in_dim(
        every_ids, lax.axis_index(("grp", "shard")), 1, keepdims=False
    )
    all_queries = lax.all_gather(queries, ("grp", "shard"), axis=0, tiled=True)
    tile = 256 if owned % 256 == 0 else owned
    updated, new_counts, partial = fused_update(
        arrived_ids.reshape(1, slot_rows),
        arrived,
        centroids,
        counts.reshape(owned, 1),
        all_queries,
        tile,
    )
    gathered = lax.all_to_all(
        partial.reshape(owners, query_rows), ("grp", "shard"), split_axis=0, concat_axis=0,
        tiled=True,
    )
    own_best = jnp.min(gathered, axis=0)
    query_norm = jnp.sum(jnp.square(queries.astype(jnp.float32)), axis=1)
    distance = (own_best + query_norm) / features
    return (updated, new_counts.reshape(owned), distance)


def solution(mesh):
    placed = (
        P(("grp", "shard"), None),
        P(("grp", "shard")),
        P(("grp", "shard"), None),
        P(("grp", "shard"), None),
        P(("grp", "shard")),
        P(("grp", "shard"), None),
    )
    return jax.shard_map(
        body,
        mesh=mesh,
        in_specs=placed,
        out_specs=(P(("grp", "shard"), None), P(("grp", "shard")), P(("grp", "shard"))),
        check_vma=False,
    )
```

```python
import functools

import jax
import jax.numpy as jnp
from jax import lax
from jax.experimental import pallas as pl
from jax.experimental.pallas import tpu as pltpu
from jax.sharding import PartitionSpec as P


def fused_kernel(ids_ref, rows_ref, cent_ref, counts_ref, q_ref, upd_ref, nc_ref, min_ref, *, tile):
    step = pl.program_id(0)
    centroid = step * tile + lax.broadcasted_iota(jnp.int32, (tile, 1), 0)
    match = ids_ref[...] == centroid
    onehot = jnp.where(match, 1.0, 0.0)
    sums = jnp.dot(
        onehot.astype(jnp.bfloat16), rows_ref[...], preferred_element_type=jnp.float32
    )
    hits = jnp.sum(onehot, axis=1, keepdims=True)
    cent = cent_ref[...]
    new_counts = counts_ref[...] + hits
    updated = cent + (sums - hits * cent) / new_counts
    upd_ref[...] = updated
    nc_ref[...] = new_counts
    rounded = updated.astype(jnp.bfloat16)
    wide = rounded.astype(jnp.float32)
    norm = jnp.sum(wide * wide, axis=1, keepdims=True)
    inner = lax.dot_general(
        rounded, q_ref[...], (((1,), (1,)), ((), ())), preferred_element_type=jnp.float32
    )
    least = jnp.min(norm - 2.0 * inner, axis=0, keepdims=True)

    @pl.when(step == 0)
    def _():
        min_ref[...] = least

    @pl.when(step > 0)
    def _():
        min_ref[...] = jnp.minimum(min_ref[...], least)


def fused_update(ids_row, rows, centroids, counts_col, all_queries, tile):
    owned, features = centroids.shape
    slots = rows.shape[0]
    query_all = all_queries.shape[0]
    steps = owned // tile
    flops = 2 * owned * slots * features + 2 * owned * query_all * features
    moved = rows.size * 2 + centroids.size * 8 + all_queries.size * 2
    return pl.pallas_call(
        functools.partial(fused_kernel, tile=tile),
        grid=(steps,),
        in_specs=[
            pl.BlockSpec((1, slots), lambda i: (0, 0)),
            pl.BlockSpec((slots, features), lambda i: (0, 0)),
            pl.BlockSpec((tile, features), lambda i: (i, 0)),
            pl.BlockSpec((tile, 1), lambda i: (i, 0)),
            pl.BlockSpec((query_all, features), lambda i: (0, 0)),
        ],
        out_specs=[
            pl.BlockSpec((tile, features), lambda i: (i, 0)),
            pl.BlockSpec((tile, 1), lambda i: (i, 0)),
            pl.BlockSpec((1, query_all), lambda i: (0, 0)),
        ],
        out_shape=[
            jax.ShapeDtypeStruct((owned, features), jnp.float32),
            jax.ShapeDtypeStruct((owned, 1), jnp.float32),
            jax.ShapeDtypeStruct((1, query_all), jnp.float32),
        ],
        compiler_params=pltpu.CompilerParams(
            dimension_semantics=("arbitrary",), vmem_limit_bytes=60 * 1024 * 1024
        ),
        cost_estimate=pl.CostEstimate(flops=flops, bytes_accessed=moved, transcendentals=0),
    )(ids_row, rows, centroids, counts_col, all_queries)


def body(points, local_ids, block_counts, centroids, counts, queries):
    groups = lax.axis_size("grp")
    shards = lax.axis_size("shard")
    owners = groups * shards
    slot_rows, features = points.shape
    capacity = slot_rows // owners
    owned = centroids.shape[0]
    query_rows = queries.shape[0]
    position = lax.broadcasted_iota(jnp.int32, (owners, capacity), 1)
    filled = block_counts.reshape(owners, 1)
    tagged = jnp.where(position < filled, local_ids.reshape(owners, capacity), -1).reshape(
        slot_rows
    )
    arrived = lax.all_to_all(points, ("grp", "shard"), split_axis=0, concat_axis=0, tiled=True)
    shifted = tagged + 1
    codes = jnp.concatenate([shifted // 64, shifted % 64]).astype(jnp.bfloat16)
    code_rows = -(-codes.shape[0] // features)
    codes = jnp.pad(codes, (0, code_rows * features - codes.shape[0]))
    payload = jnp.concatenate([queries, codes.reshape(code_rows, features)], axis=0)
    gathered = lax.all_gather(payload, ("grp", "shard"), axis=0)
    all_queries = gathered[:, :query_rows].reshape(owners * query_rows, features)
    received = gathered[:, query_rows:].reshape(owners, code_rows * features)[:, : 2 * slot_rows]
    received = received.reshape(owners, 2, owners, capacity)
    mine = lax.dynamic_index_in_dim(received, lax.axis_index(("grp", "shard")), 2, keepdims=False)
    mine = mine.astype(jnp.int32)
    arrived_ids = mine[:, 0] * 64 + mine[:, 1] - 1
    tile = 256 if owned % 256 == 0 else owned
    updated, new_counts, partial = fused_update(
        arrived_ids.reshape(1, slot_rows),
        arrived,
        centroids,
        counts.reshape(owned, 1),
        all_queries,
        tile,
    )
    gathered = lax.all_to_all(
        partial.reshape(owners, query_rows), ("grp", "shard"), split_axis=0, concat_axis=0,
        tiled=True,
    )
    own_best = jnp.min(gathered, axis=0)
    query_norm = jnp.sum(jnp.square(queries.astype(jnp.float32)), axis=1)
    distance = (own_best + query_norm) / features
    return (updated, new_counts.reshape(owned), distance)


def solution(mesh):
    placed = (
        P(("grp", "shard"), None),
        P(("grp", "shard")),
        P(("grp", "shard"), None),
        P(("grp", "shard"), None),
        P(("grp", "shard")),
        P(("grp", "shard"), None),
    )
    return jax.shard_map(
        body,
        mesh=mesh,
        in_specs=placed,
        out_specs=(P(("grp", "shard"), None), P(("grp", "shard")), P(("grp", "shard"))),
        check_vma=False,
    )
```

```python
import functools

import jax
import jax.numpy as jnp
from jax import lax
from jax.experimental import pallas as pl
from jax.experimental.pallas import tpu as pltpu
from jax.sharding import PartitionSpec as P


def fused_kernel(ids_ref, rows_ref, cent_ref, counts_ref, q_ref, upd_ref, nc_ref, min_ref, *, tile):
    step = pl.program_id(0)
    centroid = step * tile + lax.broadcasted_iota(jnp.int32, (tile, 1), 0)
    match = ids_ref[...] == centroid
    onehot = jnp.where(match, 1.0, 0.0)
    sums = jnp.dot(
        onehot.astype(jnp.bfloat16), rows_ref[...], preferred_element_type=jnp.float32
    )
    hits = jnp.sum(onehot, axis=1, keepdims=True)
    cent = cent_ref[...]
    new_counts = counts_ref[...] + hits
    updated = cent + (sums - hits * cent) / new_counts
    upd_ref[...] = updated
    nc_ref[...] = new_counts
    rounded = updated.astype(jnp.bfloat16)
    wide = rounded.astype(jnp.float32)
    norm = jnp.sum(wide * wide, axis=1, keepdims=True)
    inner = lax.dot_general(
        rounded, q_ref[...], (((1,), (1,)), ((), ())), preferred_element_type=jnp.float32
    )
    least = jnp.min(norm - 2.0 * inner, axis=0, keepdims=True)

    @pl.when(step == 0)
    def _():
        min_ref[...] = least

    @pl.when(step > 0)
    def _():
        min_ref[...] = jnp.minimum(min_ref[...], least)


def fused_update(ids_row, rows, centroids, counts_col, all_queries, tile):
    owned, features = centroids.shape
    slots = rows.shape[0]
    query_all = all_queries.shape[0]
    steps = owned // tile
    flops = 2 * owned * slots * features + 2 * owned * query_all * features
    moved = rows.size * 2 + centroids.size * 8 + all_queries.size * 2
    return pl.pallas_call(
        functools.partial(fused_kernel, tile=tile),
        grid=(steps,),
        in_specs=[
            pl.BlockSpec((1, slots), lambda i: (0, 0)),
            pl.BlockSpec((slots, features), lambda i: (0, 0)),
            pl.BlockSpec((tile, features), lambda i: (i, 0)),
            pl.BlockSpec((tile, 1), lambda i: (i, 0)),
            pl.BlockSpec((query_all, features), lambda i: (0, 0)),
        ],
        out_specs=[
            pl.BlockSpec((tile, features), lambda i: (i, 0)),
            pl.BlockSpec((tile, 1), lambda i: (i, 0)),
            pl.BlockSpec((1, query_all), lambda i: (0, 0)),
        ],
        out_shape=[
            jax.ShapeDtypeStruct((owned, features), jnp.float32),
            jax.ShapeDtypeStruct((owned, 1), jnp.float32),
            jax.ShapeDtypeStruct((1, query_all), jnp.float32),
        ],
        compiler_params=pltpu.CompilerParams(
            dimension_semantics=("arbitrary",), vmem_limit_bytes=60 * 1024 * 1024
        ),
        cost_estimate=pl.CostEstimate(flops=flops, bytes_accessed=moved, transcendentals=0),
    )(ids_row, rows, centroids, counts_col, all_queries)


def body(points, local_ids, block_counts, centroids, counts, queries):
    groups = lax.axis_size("grp")
    shards = lax.axis_size("shard")
    owners = groups * shards
    slot_rows, features = points.shape
    capacity = slot_rows // owners
    owned = centroids.shape[0]
    query_rows = queries.shape[0]
    position = lax.broadcasted_iota(jnp.int32, (owners, capacity), 1)
    filled = block_counts.reshape(owners, 1)
    tagged = jnp.where(position < filled, local_ids.reshape(owners, capacity), -1).reshape(
        slot_rows
    )
    arrived = lax.all_to_all(points, ("grp", "shard"), split_axis=0, concat_axis=0, tiled=True)
    shifted = tagged + 1
    codes = jnp.concatenate([shifted // 64, shifted % 64]).astype(jnp.bfloat16)
    code_rows = -(-codes.shape[0] // features)
    codes = jnp.pad(codes, (0, code_rows * features - codes.shape[0]))
    payload = jnp.concatenate([queries, codes.reshape(code_rows, features)], axis=0)
    gathered = lax.all_gather(payload, ("grp", "shard"), axis=0)
    all_queries = gathered[:, :query_rows].reshape(owners * query_rows, features)
    received = gathered[:, query_rows:].reshape(owners, code_rows * features)[:, : 2 * slot_rows]
    received = received.reshape(owners, 2, owners, capacity)
    mine = lax.dynamic_index_in_dim(received, lax.axis_index(("grp", "shard")), 2, keepdims=False)
    mine = mine.astype(jnp.int32)
    arrived_ids = mine[:, 0] * 64 + mine[:, 1] - 1
    tile = 512 if owned % 512 == 0 else owned
    updated, new_counts, partial = fused_update(
        arrived_ids.reshape(1, slot_rows),
        arrived,
        centroids,
        counts.reshape(owned, 1),
        all_queries,
        tile,
    )
    gathered = lax.all_to_all(
        partial.reshape(owners, query_rows), ("grp", "shard"), split_axis=0, concat_axis=0,
        tiled=True,
    )
    own_best = jnp.min(gathered, axis=0)
    query_norm = jnp.sum(jnp.square(queries.astype(jnp.float32)), axis=1)
    distance = (own_best + query_norm) / features
    return (updated, new_counts.reshape(owned), distance)


def solution(mesh):
    placed = (
        P(("grp", "shard"), None),
        P(("grp", "shard")),
        P(("grp", "shard"), None),
        P(("grp", "shard"), None),
        P(("grp", "shard")),
        P(("grp", "shard"), None),
    )
    return jax.shard_map(
        body,
        mesh=mesh,
        in_specs=placed,
        out_specs=(P(("grp", "shard"), None), P(("grp", "shard")), P(("grp", "shard"))),
        check_vma=False,
    )
```

```python
import functools

import jax
import jax.numpy as jnp
from jax import lax
from jax.experimental import pallas as pl
from jax.experimental.pallas import tpu as pltpu
from jax.sharding import PartitionSpec as P


def fused_kernel(ids_ref, rows_ref, cent_ref, counts_ref, q_ref, upd_ref, nc_ref, min_ref, run_ref, *, tile):
    step = pl.program_id(0)
    centroid = step * tile + lax.broadcasted_iota(jnp.int32, (tile, 1), 0)
    match = ids_ref[...] == centroid
    onehot = jnp.where(match, 1.0, 0.0)
    sums = jnp.dot(
        onehot.astype(jnp.bfloat16), rows_ref[...], preferred_element_type=jnp.float32
    )
    hits = jnp.sum(onehot, axis=1, keepdims=True)
    cent = cent_ref[...]
    new_counts = counts_ref[...] + hits
    updated = cent + (sums - hits * cent) / new_counts
    upd_ref[...] = updated
    nc_ref[...] = new_counts
    rounded = updated.astype(jnp.bfloat16)
    wide = rounded.astype(jnp.float32)
    norm = jnp.sum(wide * wide, axis=1, keepdims=True)
    inner = lax.dot_general(
        rounded, q_ref[...], (((1,), (1,)), ((), ())), preferred_element_type=jnp.float32
    )
    least = jnp.min(norm - 2.0 * inner, axis=0, keepdims=True)

    @pl.when(step == 0)
    def _():
        run_ref[...] = least

    @pl.when(step > 0)
    def _():
        run_ref[...] = jnp.minimum(run_ref[...], least)

    @pl.when(step == pl.num_programs(0) - 1)
    def _():
        owners, _, query_rows = min_ref.shape
        for owner in range(owners):
            min_ref[owner] = run_ref[:, owner * query_rows : (owner + 1) * query_rows]


def fused_update(ids_row, rows, centroids, counts_col, all_queries, tile, owners):
    owned, features = centroids.shape
    slots = rows.shape[0]
    query_all = all_queries.shape[0]
    steps = owned // tile
    flops = 2 * owned * slots * features + 2 * owned * query_all * features
    moved = rows.size * 2 + centroids.size * 8 + all_queries.size * 2
    return pl.pallas_call(
        functools.partial(fused_kernel, tile=tile),
        grid=(steps,),
        in_specs=[
            pl.BlockSpec((1, slots), lambda i: (0, 0)),
            pl.BlockSpec((slots, features), lambda i: (0, 0)),
            pl.BlockSpec((tile, features), lambda i: (i, 0)),
            pl.BlockSpec((tile, 1), lambda i: (i, 0)),
            pl.BlockSpec((query_all, features), lambda i: (0, 0)),
        ],
        out_specs=[
            pl.BlockSpec((tile, features), lambda i: (i, 0)),
            pl.BlockSpec((tile, 1), lambda i: (i, 0)),
            pl.BlockSpec((owners, 1, query_all // owners), lambda i: (0, 0, 0)),
        ],
        out_shape=[
            jax.ShapeDtypeStruct((owned, features), jnp.float32),
            jax.ShapeDtypeStruct((owned, 1), jnp.float32),
            jax.ShapeDtypeStruct((owners, 1, query_all // owners), jnp.float32),
        ],
        scratch_shapes=[pltpu.VMEM((1, query_all), jnp.float32)],
        compiler_params=pltpu.CompilerParams(
            dimension_semantics=("arbitrary",), vmem_limit_bytes=60 * 1024 * 1024
        ),
        cost_estimate=pl.CostEstimate(flops=flops, bytes_accessed=moved, transcendentals=0),
    )(ids_row, rows, centroids, counts_col, all_queries)


def body(points, local_ids, block_counts, centroids, counts, queries):
    groups = lax.axis_size("grp")
    shards = lax.axis_size("shard")
    owners = groups * shards
    slot_rows, features = points.shape
    capacity = slot_rows // owners
    owned = centroids.shape[0]
    query_rows = queries.shape[0]
    position = lax.broadcasted_iota(jnp.int32, (owners, capacity), 1)
    filled = block_counts.reshape(owners, 1)
    tagged = jnp.where(position < filled, local_ids.reshape(owners, capacity), -1).reshape(
        slot_rows
    )
    arrived = lax.all_to_all(points, ("grp", "shard"), split_axis=0, concat_axis=0, tiled=True)
    shifted = tagged + 1
    codes = jnp.concatenate([shifted // 64, shifted % 64]).astype(jnp.bfloat16)
    code_rows = -(-codes.shape[0] // features)
    codes = jnp.pad(codes, (0, code_rows * features - codes.shape[0]))
    payload = jnp.concatenate([queries, codes.reshape(code_rows, features)], axis=0)
    gathered = lax.all_gather(payload, ("grp", "shard"), axis=0)
    all_queries = gathered[:, :query_rows].reshape(owners * query_rows, features)
    received = gathered[:, query_rows:].reshape(owners, code_rows * features)[:, : 2 * slot_rows]
    received = received.reshape(owners, 2, owners, capacity)
    mine = lax.dynamic_index_in_dim(received, lax.axis_index(("grp", "shard")), 2, keepdims=False)
    mine = mine.astype(jnp.int32)
    arrived_ids = mine[:, 0] * 64 + mine[:, 1] - 1
    tile = 512 if owned % 512 == 0 else owned
    updated, new_counts, partial = fused_update(
        arrived_ids.reshape(1, slot_rows),
        arrived,
        centroids,
        counts.reshape(owned, 1),
        all_queries,
        tile,
        owners,
    )
    exchanged = lax.all_to_all(partial, ("grp", "shard"), split_axis=0, concat_axis=0, tiled=True)
    own_best = jnp.min(exchanged, axis=(0, 1))
    query_norm = jnp.sum(jnp.square(queries.astype(jnp.float32)), axis=1)
    distance = (own_best + query_norm) / features
    return (updated, new_counts.reshape(owned), distance)


def solution(mesh):
    placed = (
        P(("grp", "shard"), None),
        P(("grp", "shard")),
        P(("grp", "shard"), None),
        P(("grp", "shard"), None),
        P(("grp", "shard")),
        P(("grp", "shard"), None),
    )
    return jax.shard_map(
        body,
        mesh=mesh,
        in_specs=placed,
        out_specs=(P(("grp", "shard"), None), P(("grp", "shard")), P(("grp", "shard"))),
        check_vma=False,
    )
```

```python
import functools

import jax
import jax.numpy as jnp
from jax import lax
from jax.experimental import pallas as pl
from jax.experimental.pallas import tpu as pltpu
from jax.sharding import PartitionSpec as P


def fused_kernel(ids_ref, rows_ref, cent_ref, counts_ref, q_ref, upd_ref, nc_ref, min_ref, run_ref, *, tile):
    step = pl.program_id(0)
    centroid = step * tile + lax.broadcasted_iota(jnp.int32, (tile, 1), 0)
    match = ids_ref[...] == centroid
    onehot = jnp.where(match, 1.0, 0.0)
    sums = jnp.dot(
        onehot.astype(jnp.bfloat16), rows_ref[...], preferred_element_type=jnp.float32
    )
    hits = jnp.sum(onehot, axis=1, keepdims=True)
    cent = cent_ref[...]
    new_counts = counts_ref[...] + hits
    updated = cent + (sums - hits * cent) / new_counts
    upd_ref[...] = updated
    nc_ref[...] = new_counts
    rounded = updated.astype(jnp.bfloat16)
    wide = rounded.astype(jnp.float32)
    norm = jnp.sum(wide * wide, axis=1, keepdims=True)
    inner = lax.dot_general(
        rounded, q_ref[...], (((1,), (1,)), ((), ())), preferred_element_type=jnp.float32
    )
    least = jnp.min(norm - 2.0 * inner, axis=0, keepdims=True)

    @pl.when(step == 0)
    def _():
        run_ref[...] = least

    @pl.when(step > 0)
    def _():
        run_ref[...] = jnp.minimum(run_ref[...], least)

    @pl.when(step == pl.num_programs(0) - 1)
    def _():
        owners, _, query_rows = min_ref.shape
        for owner in range(owners):
            min_ref[owner] = run_ref[:, owner * query_rows : (owner + 1) * query_rows]


def fused_update(ids_row, rows, centroids, counts_col, all_queries, tile, owners):
    owned, features = centroids.shape
    slots = rows.shape[0]
    query_all = all_queries.shape[0]
    steps = owned // tile
    flops = 2 * owned * slots * features + 2 * owned * query_all * features
    moved = rows.size * 2 + centroids.size * 8 + all_queries.size * 2
    return pl.pallas_call(
        functools.partial(fused_kernel, tile=tile),
        grid=(steps,),
        in_specs=[
            pl.BlockSpec((1, slots), lambda i: (0, 0)),
            pl.BlockSpec(memory_space=pltpu.VMEM),
            pl.BlockSpec((tile, features), lambda i: (i, 0)),
            pl.BlockSpec((tile, 1), lambda i: (i, 0)),
            pl.BlockSpec((query_all, features), lambda i: (0, 0)),
        ],
        out_specs=[
            pl.BlockSpec((tile, features), lambda i: (i, 0)),
            pl.BlockSpec((tile, 1), lambda i: (i, 0)),
            pl.BlockSpec((owners, 1, query_all // owners), lambda i: (0, 0, 0)),
        ],
        out_shape=[
            jax.ShapeDtypeStruct((owned, features), jnp.float32),
            jax.ShapeDtypeStruct((owned, 1), jnp.float32),
            jax.ShapeDtypeStruct((owners, 1, query_all // owners), jnp.float32),
        ],
        scratch_shapes=[pltpu.VMEM((1, query_all), jnp.float32)],
        compiler_params=pltpu.CompilerParams(
            dimension_semantics=("arbitrary",), vmem_limit_bytes=60 * 1024 * 1024
        ),
        cost_estimate=pl.CostEstimate(flops=flops, bytes_accessed=moved, transcendentals=0),
    )(ids_row, rows, centroids, counts_col, all_queries)


def body(points, local_ids, block_counts, centroids, counts, queries):
    groups = lax.axis_size("grp")
    shards = lax.axis_size("shard")
    owners = groups * shards
    slot_rows, features = points.shape
    capacity = slot_rows // owners
    owned = centroids.shape[0]
    query_rows = queries.shape[0]
    position = lax.broadcasted_iota(jnp.int32, (owners, capacity), 1)
    filled = block_counts.reshape(owners, 1)
    tagged = jnp.where(position < filled, local_ids.reshape(owners, capacity), -1).reshape(
        slot_rows
    )
    arrived = lax.all_to_all(points, ("grp", "shard"), split_axis=0, concat_axis=0, tiled=True)
    shifted = tagged + 1
    codes = jnp.concatenate([shifted // 64, shifted % 64]).astype(jnp.bfloat16)
    code_rows = -(-codes.shape[0] // features)
    codes = jnp.pad(codes, (0, code_rows * features - codes.shape[0]))
    payload = jnp.concatenate([queries, codes.reshape(code_rows, features)], axis=0)
    gathered = lax.all_gather(payload, ("grp", "shard"), axis=0)
    all_queries = gathered[:, :query_rows].reshape(owners * query_rows, features)
    received = gathered[:, query_rows:].reshape(owners, code_rows * features)[:, : 2 * slot_rows]
    received = received.reshape(owners, 2, owners, capacity)
    mine = lax.dynamic_index_in_dim(received, lax.axis_index(("grp", "shard")), 2, keepdims=False)
    mine = mine.astype(jnp.int32)
    arrived_ids = mine[:, 0] * 64 + mine[:, 1] - 1
    tile = 512 if owned % 512 == 0 else owned
    updated, new_counts, partial = fused_update(
        arrived_ids.reshape(1, slot_rows),
        pltpu.with_memory_space_constraint(arrived, pltpu.VMEM),
        centroids,
        counts.reshape(owned, 1),
        all_queries,
        tile,
        owners,
    )
    exchanged = lax.all_to_all(partial, ("grp", "shard"), split_axis=0, concat_axis=0, tiled=True)
    own_best = jnp.min(exchanged, axis=(0, 1))
    query_norm = jnp.sum(jnp.square(queries.astype(jnp.float32)), axis=1)
    distance = (own_best + query_norm) / features
    return (updated, new_counts.reshape(owned), distance)


def solution(mesh):
    placed = (
        P(("grp", "shard"), None),
        P(("grp", "shard")),
        P(("grp", "shard"), None),
        P(("grp", "shard"), None),
        P(("grp", "shard")),
        P(("grp", "shard"), None),
    )
    return jax.shard_map(
        body,
        mesh=mesh,
        in_specs=placed,
        out_specs=(P(("grp", "shard"), None), P(("grp", "shard")), P(("grp", "shard"))),
        check_vma=False,
    )
```

```python
import functools

import jax
import jax.numpy as jnp
from jax import lax
from jax.experimental import pallas as pl
from jax.experimental.pallas import tpu as pltpu
from jax.sharding import PartitionSpec as P


def fused_kernel(ids_ref, rows_ref, cent_ref, counts_ref, q_ref, upd_ref, nc_ref, min_ref, run_ref, *, tile):
    step = pl.program_id(0)
    centroid = step * tile + lax.broadcasted_iota(jnp.int32, (tile, 1), 0)
    match = ids_ref[...] == centroid
    onehot = jnp.where(match, 1.0, 0.0)
    sums = jnp.dot(
        onehot.astype(jnp.bfloat16), rows_ref[...], preferred_element_type=jnp.float32
    )
    hits = jnp.sum(onehot, axis=1, keepdims=True)
    cent = cent_ref[...]
    new_counts = counts_ref[...] + hits
    scale = 1.0 / new_counts
    updated = cent + (sums - hits * cent) * scale
    upd_ref[...] = updated
    nc_ref[...] = new_counts
    rounded = updated.astype(jnp.bfloat16)
    wide = rounded.astype(jnp.float32)
    norm = jnp.sum(wide * wide, axis=1, keepdims=True)
    inner = lax.dot_general(
        rounded, q_ref[...], (((1,), (1,)), ((), ())), preferred_element_type=jnp.float32
    )
    least = jnp.min(norm - 2.0 * inner, axis=0, keepdims=True)

    @pl.when(step == 0)
    def _():
        run_ref[...] = least

    @pl.when(step > 0)
    def _():
        run_ref[...] = jnp.minimum(run_ref[...], least)

    @pl.when(step == pl.num_programs(0) - 1)
    def _():
        owners, _, query_rows = min_ref.shape
        for owner in range(owners):
            min_ref[owner] = run_ref[:, owner * query_rows : (owner + 1) * query_rows]


def fused_update(ids_row, rows, centroids, counts_col, all_queries, tile, owners):
    owned, features = centroids.shape
    slots = rows.shape[0]
    query_all = all_queries.shape[0]
    steps = owned // tile
    flops = 2 * owned * slots * features + 2 * owned * query_all * features
    moved = rows.size * 2 + centroids.size * 8 + all_queries.size * 2
    return pl.pallas_call(
        functools.partial(fused_kernel, tile=tile),
        grid=(steps,),
        in_specs=[
            pl.BlockSpec((1, slots), lambda i: (0, 0)),
            pl.BlockSpec(memory_space=pltpu.VMEM),
            pl.BlockSpec((tile, features), lambda i: (i, 0)),
            pl.BlockSpec((tile, 1), lambda i: (i, 0)),
            pl.BlockSpec((query_all, features), lambda i: (0, 0)),
        ],
        out_specs=[
            pl.BlockSpec((tile, features), lambda i: (i, 0)),
            pl.BlockSpec((tile, 1), lambda i: (i, 0)),
            pl.BlockSpec((owners, 1, query_all // owners), lambda i: (0, 0, 0)),
        ],
        out_shape=[
            jax.ShapeDtypeStruct((owned, features), jnp.float32),
            jax.ShapeDtypeStruct((owned, 1), jnp.float32),
            jax.ShapeDtypeStruct((owners, 1, query_all // owners), jnp.float32),
        ],
        scratch_shapes=[pltpu.VMEM((1, query_all), jnp.float32)],
        compiler_params=pltpu.CompilerParams(
            dimension_semantics=("arbitrary",), vmem_limit_bytes=60 * 1024 * 1024
        ),
        cost_estimate=pl.CostEstimate(flops=flops, bytes_accessed=moved, transcendentals=0),
    )(ids_row, rows, centroids, counts_col, all_queries)


def body(points, local_ids, block_counts, centroids, counts, queries):
    groups = lax.axis_size("grp")
    shards = lax.axis_size("shard")
    owners = groups * shards
    slot_rows, features = points.shape
    capacity = slot_rows // owners
    owned = centroids.shape[0]
    query_rows = queries.shape[0]
    position = lax.broadcasted_iota(jnp.int32, (owners, capacity), 1)
    filled = block_counts.reshape(owners, 1)
    tagged = jnp.where(position < filled, local_ids.reshape(owners, capacity), -1).reshape(
        slot_rows
    )
    arrived = lax.all_to_all(points, ("grp", "shard"), split_axis=0, concat_axis=0, tiled=True)
    shifted = tagged + 1
    codes = jnp.concatenate([shifted // 64, shifted % 64]).astype(jnp.bfloat16)
    code_rows = -(-codes.shape[0] // features)
    codes = jnp.pad(codes, (0, code_rows * features - codes.shape[0]))
    payload = jnp.concatenate([queries, codes.reshape(code_rows, features)], axis=0)
    gathered = lax.all_gather(payload, ("grp", "shard"), axis=0)
    all_queries = gathered[:, :query_rows].reshape(owners * query_rows, features)
    received = gathered[:, query_rows:].reshape(owners, code_rows * features)[:, : 2 * slot_rows]
    received = received.reshape(owners, 2, owners, capacity)
    mine = lax.dynamic_index_in_dim(received, lax.axis_index(("grp", "shard")), 2, keepdims=False)
    mine = mine.astype(jnp.int32)
    arrived_ids = mine[:, 0] * 64 + mine[:, 1] - 1
    tile = 512 if owned % 512 == 0 else owned
    updated, new_counts, partial = fused_update(
        arrived_ids.reshape(1, slot_rows),
        pltpu.with_memory_space_constraint(arrived, pltpu.VMEM),
        centroids,
        counts.reshape(owned, 1),
        all_queries,
        tile,
        owners,
    )
    exchanged = lax.all_to_all(partial, ("grp", "shard"), split_axis=0, concat_axis=0, tiled=True)
    own_best = jnp.min(exchanged, axis=(0, 1))
    query_norm = jnp.sum(jnp.square(queries.astype(jnp.float32)), axis=1)
    distance = (own_best + query_norm) / features
    return (updated, new_counts.reshape(owned), distance)


def solution(mesh):
    placed = (
        P(("grp", "shard"), None),
        P(("grp", "shard")),
        P(("grp", "shard"), None),
        P(("grp", "shard"), None),
        P(("grp", "shard")),
        P(("grp", "shard"), None),
    )
    return jax.shard_map(
        body,
        mesh=mesh,
        in_specs=placed,
        out_specs=(P(("grp", "shard"), None), P(("grp", "shard")), P(("grp", "shard"))),
        check_vma=False,
    )
```

```python
import functools

import jax
import jax.numpy as jnp
from jax import lax
from jax.experimental import pallas as pl
from jax.experimental.pallas import tpu as pltpu
from jax.sharding import PartitionSpec as P


def fused_kernel(ids_ref, rows_ref, cent_ref, counts_ref, q_ref, upd_ref, nc_ref, min_ref, run_ref, *, tile):
    step = pl.program_id(0)
    centroid = step * tile + lax.broadcasted_iota(jnp.int32, (tile, 1), 0)
    match = ids_ref[...] == centroid
    onehot = jnp.where(match, 1.0, 0.0)
    sums = jnp.dot(
        onehot.astype(jnp.bfloat16), rows_ref[...], preferred_element_type=jnp.float32
    )
    hits = jnp.sum(onehot, axis=1, keepdims=True)
    cent = cent_ref[...]
    new_counts = counts_ref[...] + hits
    updated = cent + (sums - hits * cent) / new_counts
    upd_ref[...] = updated
    nc_ref[...] = new_counts
    rounded = updated.astype(jnp.bfloat16)
    wide = rounded.astype(jnp.float32)
    norm = jnp.sum(wide * wide, axis=1, keepdims=True)
    inner = lax.dot_general(
        rounded, q_ref[...], (((1,), (1,)), ((), ())), preferred_element_type=jnp.float32
    )
    least = jnp.min(norm - 2.0 * inner, axis=0, keepdims=True)

    @pl.when(step == 0)
    def _():
        run_ref[...] = least

    @pl.when(step > 0)
    def _():
        run_ref[...] = jnp.minimum(run_ref[...], least)

    @pl.when(step == pl.num_programs(0) - 1)
    def _():
        owners, _, query_rows = min_ref.shape
        for owner in range(owners):
            min_ref[owner] = run_ref[:, owner * query_rows : (owner + 1) * query_rows]


def fused_update(ids_row, rows, centroids, counts_col, all_queries, tile, owners):
    owned, features = centroids.shape
    slots = rows.shape[0]
    query_all = all_queries.shape[0]
    steps = owned // tile
    flops = 2 * owned * slots * features + 2 * owned * query_all * features
    moved = rows.size * 2 + centroids.size * 8 + all_queries.size * 2
    return pl.pallas_call(
        functools.partial(fused_kernel, tile=tile),
        grid=(steps,),
        in_specs=[
            pl.BlockSpec((1, slots), lambda i: (0, 0)),
            pl.BlockSpec(memory_space=pltpu.VMEM),
            pl.BlockSpec((tile, features), lambda i: (i, 0)),
            pl.BlockSpec((tile, 1), lambda i: (i, 0)),
            pl.BlockSpec((query_all, features), lambda i: (0, 0)),
        ],
        out_specs=[
            pl.BlockSpec((tile, features), lambda i: (i, 0)),
            pl.BlockSpec((tile, 1), lambda i: (i, 0)),
            pl.BlockSpec((owners, 1, query_all // owners), lambda i: (0, 0, 0)),
        ],
        out_shape=[
            jax.ShapeDtypeStruct((owned, features), jnp.float32),
            jax.ShapeDtypeStruct((owned, 1), jnp.float32),
            jax.ShapeDtypeStruct((owners, 1, query_all // owners), jnp.float32),
        ],
        scratch_shapes=[pltpu.VMEM((1, query_all), jnp.float32)],
        compiler_params=pltpu.CompilerParams(
            dimension_semantics=("arbitrary",), vmem_limit_bytes=60 * 1024 * 1024
        ),
        cost_estimate=pl.CostEstimate(flops=flops, bytes_accessed=moved, transcendentals=0),
    )(ids_row, rows, centroids, counts_col, all_queries)


def body(points, local_ids, block_counts, centroids, counts, queries):
    groups = lax.axis_size("grp")
    shards = lax.axis_size("shard")
    owners = groups * shards
    slot_rows, features = points.shape
    capacity = slot_rows // owners
    owned = centroids.shape[0]
    query_rows = queries.shape[0]
    position = lax.broadcasted_iota(jnp.int32, (owners, capacity), 1)
    filled = block_counts.reshape(owners, 1)
    tagged = jnp.where(position < filled, local_ids.reshape(owners, capacity), -1).reshape(
        slot_rows
    )
    arrived = lax.all_to_all(points, ("grp", "shard"), split_axis=0, concat_axis=0, tiled=True)
    shifted = tagged + 1
    level, offset = shifted // 128, shifted % 128
    up = jnp.asarray([2.0 ** (k - 7) for k in range(17)], jnp.float32)
    codes = ((offset + 128).astype(jnp.float32) * up[level]).astype(jnp.bfloat16)
    code_rows = -(-codes.shape[0] // features)
    codes = jnp.pad(codes, (0, code_rows * features - codes.shape[0]))
    payload = jnp.concatenate([queries, codes.reshape(code_rows, features)], axis=0)
    gathered = lax.all_gather(payload, ("grp", "shard"), axis=0)
    all_queries = gathered[:, :query_rows].reshape(owners * query_rows, features)
    received = gathered[:, query_rows:].reshape(owners, code_rows * features)[:, :slot_rows]
    received = received.reshape(owners, owners, capacity)
    mine = lax.dynamic_index_in_dim(received, lax.axis_index(("grp", "shard")), 1, keepdims=False)
    mine = mine.astype(jnp.float32)
    found = sum((mine >= 2.0**k).astype(jnp.int32) for k in range(1, 17))
    down = jnp.asarray([2.0 ** (7 - k) for k in range(17)], jnp.float32)
    arrived_ids = found * 128 + (mine * down[found]).astype(jnp.int32) - 128 - 1
    tile = 512 if owned % 512 == 0 else owned
    updated, new_counts, partial = fused_update(
        arrived_ids.reshape(1, slot_rows),
        pltpu.with_memory_space_constraint(arrived, pltpu.VMEM),
        centroids,
        counts.reshape(owned, 1),
        all_queries,
        tile,
        owners,
    )
    exchanged = lax.all_to_all(partial, ("grp", "shard"), split_axis=0, concat_axis=0, tiled=True)
    own_best = jnp.min(exchanged, axis=(0, 1))
    query_norm = jnp.sum(jnp.square(queries.astype(jnp.float32)), axis=1)
    distance = (own_best + query_norm) / features
    return (updated, new_counts.reshape(owned), distance)


def solution(mesh):
    placed = (
        P(("grp", "shard"), None),
        P(("grp", "shard")),
        P(("grp", "shard"), None),
        P(("grp", "shard"), None),
        P(("grp", "shard")),
        P(("grp", "shard"), None),
    )
    return jax.shard_map(
        body,
        mesh=mesh,
        in_specs=placed,
        out_specs=(P(("grp", "shard"), None), P(("grp", "shard")), P(("grp", "shard"))),
        check_vma=False,
    )
```

```python
import functools

import jax
import jax.numpy as jnp
from jax import lax
from jax.experimental import pallas as pl
from jax.experimental.pallas import tpu as pltpu
from jax.sharding import PartitionSpec as P


def fused_kernel(ids_ref, rows_ref, cent_ref, counts_ref, q_ref, upd_ref, nc_ref, min_ref, run_ref, *, tile):
    step = pl.program_id(0)
    centroid = step * tile + lax.broadcasted_iota(jnp.int32, (tile, 1), 0)
    match = ids_ref[...] == centroid
    onehot = jnp.where(match, 1.0, 0.0)
    sums = jnp.dot(
        onehot.astype(jnp.bfloat16), rows_ref[...], preferred_element_type=jnp.float32
    )
    hits = jnp.sum(onehot, axis=1, keepdims=True)
    cent = cent_ref[...]
    new_counts = counts_ref[...] + hits
    updated = cent + (sums - hits * cent) / new_counts
    upd_ref[...] = updated
    nc_ref[...] = new_counts
    rounded = updated.astype(jnp.bfloat16)
    wide = rounded.astype(jnp.float32)
    norm = jnp.sum(wide * wide, axis=1, keepdims=True)
    inner = lax.dot_general(
        rounded,
        q_ref[...].reshape(-1, q_ref.shape[2]),
        (((1,), (1,)), ((), ())),
        preferred_element_type=jnp.float32,
    )
    least = jnp.min(norm - 2.0 * inner, axis=0, keepdims=True)

    @pl.when(step == 0)
    def _():
        run_ref[...] = least

    @pl.when(step > 0)
    def _():
        run_ref[...] = jnp.minimum(run_ref[...], least)

    @pl.when(step == pl.num_programs(0) - 1)
    def _():
        owners, _, query_rows = min_ref.shape
        for owner in range(owners):
            min_ref[owner] = run_ref[:, owner * query_rows : (owner + 1) * query_rows]


def fused_update(ids_row, rows, centroids, counts_col, gathered, query_rows, tile):
    owned, features = centroids.shape
    slots = rows.shape[0]
    owners = gathered.shape[0]
    query_all = owners * query_rows
    steps = owned // tile
    flops = 2 * owned * slots * features + 2 * owned * query_all * features
    moved = rows.size * 2 + centroids.size * 8 + query_all * features * 2
    return pl.pallas_call(
        functools.partial(fused_kernel, tile=tile),
        grid=(steps,),
        in_specs=[
            pl.BlockSpec((1, slots), lambda i: (0, 0)),
            pl.BlockSpec(memory_space=pltpu.VMEM),
            pl.BlockSpec((tile, features), lambda i: (i, 0)),
            pl.BlockSpec((tile, 1), lambda i: (i, 0)),
            pl.BlockSpec((owners, query_rows, features), lambda i: (0, 0, 0)),
        ],
        out_specs=[
            pl.BlockSpec((tile, features), lambda i: (i, 0)),
            pl.BlockSpec((tile, 1), lambda i: (i, 0)),
            pl.BlockSpec((owners, 1, query_all // owners), lambda i: (0, 0, 0)),
        ],
        out_shape=[
            jax.ShapeDtypeStruct((owned, features), jnp.float32),
            jax.ShapeDtypeStruct((owned, 1), jnp.float32),
            jax.ShapeDtypeStruct((owners, 1, query_all // owners), jnp.float32),
        ],
        scratch_shapes=[pltpu.VMEM((1, query_all), jnp.float32)],
        compiler_params=pltpu.CompilerParams(
            dimension_semantics=("arbitrary",), vmem_limit_bytes=60 * 1024 * 1024
        ),
        cost_estimate=pl.CostEstimate(flops=flops, bytes_accessed=moved, transcendentals=0),
    )(ids_row, rows, centroids, counts_col, gathered)


def body(points, local_ids, block_counts, centroids, counts, queries):
    groups = lax.axis_size("grp")
    shards = lax.axis_size("shard")
    owners = groups * shards
    slot_rows, features = points.shape
    capacity = slot_rows // owners
    owned = centroids.shape[0]
    query_rows = queries.shape[0]
    position = lax.broadcasted_iota(jnp.int32, (owners, capacity), 1)
    filled = block_counts.reshape(owners, 1)
    tagged = jnp.where(position < filled, local_ids.reshape(owners, capacity), -1).reshape(
        slot_rows
    )
    arrived = lax.all_to_all(points, ("grp", "shard"), split_axis=0, concat_axis=0, tiled=True)
    shifted = tagged + 1
    codes = jnp.concatenate([shifted // 64, shifted % 64]).astype(jnp.bfloat16)
    code_rows = -(-codes.shape[0] // features)
    codes = jnp.pad(codes, (0, code_rows * features - codes.shape[0]))
    payload = jnp.concatenate([queries, codes.reshape(code_rows, features)], axis=0)
    gathered = lax.all_gather(payload, ("grp", "shard"), axis=0)
    received = gathered[:, query_rows:].reshape(owners, code_rows * features)[:, : 2 * slot_rows]
    received = received.reshape(owners, 2, owners, capacity)
    mine = lax.dynamic_index_in_dim(received, lax.axis_index(("grp", "shard")), 2, keepdims=False)
    mine = mine.astype(jnp.int32)
    arrived_ids = mine[:, 0] * 64 + mine[:, 1] - 1
    tile = 512 if owned % 512 == 0 else owned
    updated, new_counts, partial = fused_update(
        arrived_ids.reshape(1, slot_rows),
        pltpu.with_memory_space_constraint(arrived, pltpu.VMEM),
        centroids,
        counts.reshape(owned, 1),
        gathered,
        query_rows,
        tile,
    )
    exchanged = lax.all_to_all(partial, ("grp", "shard"), split_axis=0, concat_axis=0, tiled=True)
    own_best = jnp.min(exchanged, axis=(0, 1))
    query_norm = jnp.sum(jnp.square(queries.astype(jnp.float32)), axis=1)
    distance = (own_best + query_norm) / features
    return (updated, new_counts.reshape(owned), distance)


def solution(mesh):
    placed = (
        P(("grp", "shard"), None),
        P(("grp", "shard")),
        P(("grp", "shard"), None),
        P(("grp", "shard"), None),
        P(("grp", "shard")),
        P(("grp", "shard"), None),
    )
    return jax.shard_map(
        body,
        mesh=mesh,
        in_specs=placed,
        out_specs=(P(("grp", "shard"), None), P(("grp", "shard")), P(("grp", "shard"))),
        check_vma=False,
    )
```
